512 devices in a mesh: blk: 64 (over x, z, y_hi), dp: 8 (over y_lo, core).
Axes of the slice: x: 4, y: 8 (y_hi: 2, y_lo: 4; y = y_hi * 4 + y_lo), z: 8, core: 2. Of those that a mesh axis runs over, the one named last changes fastest.
Arguments:
- input_field: bfloat16 [262144, 2048], P('blk', 'dp'), may hold values from -6 to 6
- target_field: bfloat16 [262144, 2048], P('blk', 'dp'), may hold values from -6 to 6
- first_factor: bfloat16 [256, 1024, 256], P('dp', 'blk'), may hold values from -0.375 to 0.375
- second_factor: bfloat16 [256, 1024, 256], P('dp', 'blk'), may hold values from -0.375 to 0.375
Outputs:
- first_grad: bfloat16 [256, 1024, 256], P('dp', 'blk')
- second_grad: bfloat16 [256, 1024, 256], P('dp', 'blk')
The draws below stay inside these ranges and needn't reach their ends.
All inputs are finite; a program needn't handle non-finite values.
Results may differ from the reference program's by a relative error of at most 0.012.
Values may be sent and summed in bfloat16 or wider, within the bound.
No kernel may reach another device: no remote copies, remote signals or barrier semaphores. Data moves between devices by JAX's collectives and lax.ppermute only.
A program may use at most 64 MiB of HBM per device.

```python
import math
import jax
import jax.numpy as jnp
from jax import lax

NB = 1024
BS = 256
ROWS_DEV = 256
GROUPS = 4
ROWS = 2048
WIDTH = 262144
N_DP = 8


def level_of(stream_key, extent, cuts, smallest, top_value):
    loudness = 1.0
    for position, shards_of in cuts:
        draws = jax.random.uniform(jax.random.fold_in(jax.random.fold_in(stream_key, 6), position), (shards_of,), jnp.float32, smallest / len(cuts), top_value / len(cuts))
        loudness = loudness * jnp.repeat(jnp.exp(draws), extent[position] // shards_of).reshape((-1,) + (1,) * (len(extent) - 1 - position))
    return loudness


def bell_draw(own_key, shape, scale, reach, split=(), held_as=jnp.bfloat16):
    entries = scale * jax.random.normal(own_key, shape, jnp.float32)
    if split:
        entries = entries * level_of(own_key, shape, split, -0.22, 0.18)
    return jnp.clip(entries, -reach, reach).astype(held_as)


def setup_inputs(seed: int = 0) -> dict:
    streams_of = jax.random.split(jax.random.key(seed), 5)
    input_field = bell_draw(streams_of[0], (WIDTH, ROWS), 1.0, 6.0, ((0, 64), (1, 8)))
    target_field = bell_draw(streams_of[1], (WIDTH, ROWS), 1.0, 6.0, ((0, 64), (1, 8)))
    first_factor = bell_draw(streams_of[2], (BS, NB, BS), BS ** -0.5, 0.375, ((0, 8), (1, 64)))
    second_factor = bell_draw(streams_of[3], (BS, NB, BS), BS ** -0.5, 0.375, ((0, 8), (1, 64)))
    return {"input_field": input_field, "target_field": target_field, "first_factor": first_factor, "second_factor": second_factor}


tanh_scale = 0.7978845608028654
cubic_coef = 0.044715

def gelu_value(values):
    inner = jnp.tanh(tanh_scale * (values + cubic_coef * values * values * values))
    return 0.5 * values * (1.0 + inner)

def gelu_slope(values):
    inner = jnp.tanh(tanh_scale * (values + cubic_coef * values * values * values))
    return 0.5 * (1.0 + inner) + 0.5 * values * (1.0 - inner * inner) * tanh_scale * (1.0 + 3.0 * cubic_coef * values * values)

def to_half(values):
    return lax.optimization_barrier(values.astype(jnp.bfloat16)).astype(jnp.float32)

def reference(input_field, target_field, first_factor, second_factor):
    first_full = first_factor.astype(jnp.float32)
    second_full = second_factor.astype(jnp.float32)
    scale_factor = 1.0 / math.sqrt(ROWS)

    def one_run(totals, run_index):
        first_total, second_total = totals
        begin = (run_index * ROWS_DEV).astype(jnp.int32)
        inputs = lax.dynamic_slice_in_dim(input_field, begin, ROWS_DEV, 1).astype(jnp.float32).reshape(NB, BS, ROWS_DEV)
        targets = lax.dynamic_slice_in_dim(target_field, begin, ROWS_DEV, 1).astype(jnp.float32).reshape(NB, BS, ROWS_DEV)
        pre_act = jnp.einsum('bkr,kbi->bir', inputs, first_full)
        activated = to_half(gelu_value(pre_act))
        permuted = activated.reshape(GROUPS, BS, BS, ROWS_DEV).transpose(2, 0, 1, 3).reshape(NB, BS, ROWS_DEV)
        predicted = jnp.einsum('qcr,cqj->qjr', permuted, second_full)
        residual = to_half((predicted - targets) * scale_factor)
        second_run = to_half(jnp.einsum('qcr,qjr->cqj', permuted, residual))
        permuted_grad = to_half(jnp.einsum('cqj,qjr->qcr', second_full, residual))
        activated_grad = permuted_grad.reshape(BS, GROUPS, BS, ROWS_DEV).transpose(1, 2, 0, 3).reshape(NB, BS, ROWS_DEV)
        pre_grad = to_half(activated_grad * gelu_slope(pre_act))
        first_run = to_half(jnp.einsum('bkr,bir->kbi', inputs, pre_grad))
        return ((first_total + first_run, second_total + second_run), None)
    zeros = jnp.zeros((BS, NB, BS), jnp.float32)
    totals, _ = lax.scan(one_run, (zeros, zeros), jnp.arange(N_DP, dtype=jnp.int32))
    return (totals[0].astype(jnp.bfloat16), totals[1].astype(jnp.bfloat16))
```

```python
import math

import jax
import jax.numpy as jnp
from jax import lax
from jax.experimental.layout import Layout, with_layout_constraint
from jax.sharding import Mesh
from jax.sharding import PartitionSpec as P

NB = 1024
BS = 256


tanh_scale = 0.7978845608028654
cubic_coef = 0.044715


def gelu_value(values):
    inner = jnp.tanh(tanh_scale * (values + cubic_coef * values * values * values))
    return 0.5 * values * (1.0 + inner)


def gelu_slope(values):
    inner = jnp.tanh(tanh_scale * (values + cubic_coef * values * values * values))
    return 0.5 * (1.0 + inner) + 0.5 * values * (1.0 - inner * inner) * tanh_scale * (
        1.0 + 3.0 * cubic_coef * values * values
    )


def gather_rows(piece):
    n_core = lax.axis_size("core")
    n_ylo = lax.axis_size("ylo")
    along = lax.all_gather(piece, "ylo", axis=0, tiled=True)
    both = lax.all_gather(along, "core", axis=0, tiled=False)
    rows = piece.shape[0]
    both = both.reshape((n_core, n_ylo, rows) + piece.shape[1:])
    both = jnp.swapaxes(both, 0, 1)
    return both.reshape((n_ylo * n_core * rows,) + piece.shape[1:])


def scatter_rows(term):
    n_core = lax.axis_size("core")
    me = lax.axis_index("core")
    other = lax.rem(me + 1, n_core)
    sent = lax.dynamic_index_in_dim(term, other, 0, keepdims=False)
    kept = lax.dynamic_index_in_dim(term, me, 0, keepdims=False)
    got = lax.ppermute(sent, "core", [(c, (c + 1) % n_core) for c in range(n_core)])
    half = (kept.astype(jnp.float32) + got.astype(jnp.float32)).astype(jnp.bfloat16)
    half = with_layout_constraint(half, Layout(tuple(range(half.ndim))))
    part = lax.psum_scatter(half, "ylo", scatter_dimension=0, tiled=True)
    return part.reshape(part.shape[1:])


def shards(input_field, target_field, first_factor, second_factor):
    block_count = first_factor.shape[1]
    block_size = first_factor.shape[2]
    row_count = input_field.shape[1]
    replica_count = lax.axis_size("ylo") * lax.axis_size("core")
    group_count = NB // BS
    inner_count = block_count // group_count
    scale_factor = 1.0 / math.sqrt(row_count * replica_count)
    inputs = input_field.reshape(block_count, block_size, row_count)
    first_full = gather_rows(first_factor)
    second_full = gather_rows(second_factor)
    pre_act = jnp.einsum("bkr,kbi->bir", inputs, first_full, preferred_element_type=jnp.float32)
    activated = gelu_value(pre_act).astype(jnp.bfloat16)
    received = lax.all_to_all(activated, "blk", split_axis=1, concat_axis=0, tiled=True)
    permuted = received.reshape(group_count, block_size, inner_count, row_count)
    targets = target_field.reshape(inner_count, group_count, block_size, row_count)
    count = second_full.shape[0]
    split_part = second_full.reshape(count, inner_count, group_count, block_size)
    predicted = jnp.einsum(
        "gcir,cigj->igjr", permuted, split_part, preferred_element_type=jnp.float32
    )
    residual = ((predicted - targets.astype(jnp.float32)) * scale_factor).astype(jnp.bfloat16)
    permuted_grad = jnp.einsum(
        "cigj,igjr->gcir", split_part, residual, preferred_element_type=jnp.float32
    ).astype(jnp.bfloat16)
    n_core = lax.axis_size("core")
    n_ylo = lax.axis_size("ylo")
    kk = block_size // (n_core * n_ylo)
    permuted_cm = permuted.reshape(group_count, n_ylo, n_core, kk, inner_count, row_count)
    term = jnp.einsum(
        "gyxcir,igjr->xycigj", permuted_cm, residual, preferred_element_type=jnp.float32
    )
    second_out = scatter_rows(
        term.reshape(n_core, n_ylo, kk, block_count, block_size).astype(jnp.bfloat16)
    )
    sending = permuted_grad.reshape(group_count * block_size, inner_count, row_count)
    activated_grad = lax.all_to_all(sending, "blk", split_axis=0, concat_axis=1, tiled=True)
    pre_grad = (activated_grad.astype(jnp.float32) * gelu_slope(pre_act)).astype(jnp.bfloat16)
    inputs_cm = inputs.reshape(block_count, n_ylo, n_core, kk, row_count)
    first_sum = scatter_rows(
        jnp.einsum(
            "byxkr,bir->xykbi", inputs_cm, pre_grad, preferred_element_type=jnp.float32
        ).astype(jnp.bfloat16)
    )
    return (first_sum, second_out)


def solution(mesh):
    n_blk, n_dp = mesh.devices.shape
    n_core = 2
    split_mesh = Mesh(
        mesh.devices.reshape(n_blk, n_dp // n_core, n_core), ("blk", "ylo", "core")
    )
    dp = ("ylo", "core")
    return jax.shard_map(
        shards,
        mesh=split_mesh,
        in_specs=(P("blk", dp), P("blk", dp), P(dp, "blk", None), P(dp, "blk", None)),
        out_specs=(P(dp, "blk", None), P(dp, "blk", None)),
        check_vma=False,
    )
```

```python
import math

import jax
import jax.numpy as jnp
from jax import lax
from jax.sharding import Mesh
from jax.sharding import PartitionSpec as P

NB = 1024
BS = 256


tanh_scale = 0.7978845608028654
cubic_coef = 0.044715


def gelu_value(values):
    inner = jnp.tanh(tanh_scale * (values + cubic_coef * values * values * values))
    return 0.5 * values * (1.0 + inner)


def gelu_slope(values):
    inner = jnp.tanh(tanh_scale * (values + cubic_coef * values * values * values))
    return 0.5 * (1.0 + inner) + 0.5 * values * (1.0 - inner * inner) * tanh_scale * (
        1.0 + 3.0 * cubic_coef * values * values
    )


def line_pairs(n, step):
    return [(i, i + step) for i in range(n) if 0 <= i + step < n]


def swap_pairs(n):
    return [(c, (c + 1) % n) for c in range(n)]


def gather_rows(piece):
    n_core = lax.axis_size("core")
    n_ylo = lax.axis_size("ylo")
    y = lax.axis_index("ylo")
    c = lax.axis_index("core")
    right = [piece]
    left = [piece]
    for _ in range(n_ylo - 1):
        right.append(lax.ppermute(right[-1], "ylo", line_pairs(n_ylo, 1)))
        left.append(lax.ppermute(left[-1], "ylo", line_pairs(n_ylo, -1)))
    stacked = jnp.stack(right[:0:-1] + left)
    line = lax.dynamic_slice_in_dim(stacked, n_ylo - 1 - y, n_ylo, axis=0)
    other = lax.ppermute(line, "core", swap_pairs(n_core))
    pair = jnp.where(c == 0, jnp.stack([line, other], 1), jnp.stack([other, line], 1))
    return pair.reshape((n_ylo * n_core * piece.shape[0],) + piece.shape[1:])


def scatter_rows(term):
    n_core = lax.axis_size("core")
    n_ylo = lax.axis_size("ylo")
    y = lax.axis_index("ylo")
    c = lax.axis_index("core")
    sent = lax.dynamic_index_in_dim(term, lax.rem(c + 1, n_core), 0, keepdims=False)
    kept = lax.dynamic_index_in_dim(term, c, 0, keepdims=False)
    got = lax.ppermute(sent, "core", swap_pairs(n_core))
    chip = kept.astype(jnp.float32) + got.astype(jnp.float32)
    total = lax.dynamic_index_in_dim(chip, y, 0, keepdims=False)
    for step in (1, -1):
        carry = None
        for s in range(1, n_ylo):
            dest = jnp.clip(y + step * (n_ylo - s), 0, n_ylo - 1)
            block = lax.dynamic_index_in_dim(chip, dest, 0, keepdims=False)
            if carry is not None:
                block = block + carry.astype(jnp.float32)
            carry = lax.ppermute(block.astype(jnp.bfloat16), "ylo", line_pairs(n_ylo, step))
        total = total + carry.astype(jnp.float32)
    return total.astype(jnp.bfloat16)


def shards(input_field, target_field, first_factor, second_factor):
    block_count = first_factor.shape[1]
    block_size = first_factor.shape[2]
    row_count = input_field.shape[1]
    replica_count = lax.axis_size("ylo") * lax.axis_size("core")
    group_count = NB // BS
    inner_count = block_count // group_count
    scale_factor = 1.0 / math.sqrt(row_count * replica_count)
    inputs = input_field.reshape(block_count, block_size, row_count)
    first_full = gather_rows(first_factor)
    second_full = gather_rows(second_factor)
    pre_act = jnp.einsum("bkr,kbi->bir", inputs, first_full, preferred_element_type=jnp.float32)
    activated = gelu_value(pre_act).astype(jnp.bfloat16)
    received = lax.all_to_all(activated, "blk", split_axis=1, concat_axis=0, tiled=True)
    permuted = received.reshape(group_count, block_size, inner_count, row_count)
    targets = target_field.reshape(inner_count, group_count, block_size, row_count)
    count = second_full.shape[0]
    split_part = second_full.reshape(count, inner_count, group_count, block_size)
    predicted = jnp.einsum(
        "gcir,cigj->igjr", permuted, split_part, preferred_element_type=jnp.float32
    )
    residual = ((predicted - targets.astype(jnp.float32)) * scale_factor).astype(jnp.bfloat16)
    permuted_grad = jnp.einsum(
        "cigj,igjr->gcir", split_part, residual, preferred_element_type=jnp.float32
    ).astype(jnp.bfloat16)
    n_core = lax.axis_size("core")
    n_ylo = lax.axis_size("ylo")
    kk = block_size // (n_core * n_ylo)
    permuted_cm = permuted.reshape(group_count, n_ylo, n_core, kk, inner_count, row_count)
    term = jnp.einsum(
        "gyxcir,igjr->xycigj", permuted_cm, residual, preferred_element_type=jnp.float32
    )
    second_out = scatter_rows(
        term.reshape(n_core, n_ylo, kk, block_count, block_size).astype(jnp.bfloat16)
    )
    sending = permuted_grad.reshape(group_count * block_size, inner_count, row_count)
    activated_grad = lax.all_to_all(sending, "blk", split_axis=0, concat_axis=1, tiled=True)
    pre_grad = (activated_grad.astype(jnp.float32) * gelu_slope(pre_act)).astype(jnp.bfloat16)
    inputs_cm = inputs.reshape(block_count, n_ylo, n_core, kk, row_count)
    first_sum = scatter_rows(
        jnp.einsum(
            "byxkr,bir->xykbi", inputs_cm, pre_grad, preferred_element_type=jnp.float32
        ).astype(jnp.bfloat16)
    )
    return (first_sum, second_out)


def solution(mesh):
    n_blk, n_dp = mesh.devices.shape
    n_core = 2
    split_mesh = Mesh(
        mesh.devices.reshape(n_blk, n_dp // n_core, n_core), ("blk", "ylo", "core")
    )
    dp = ("ylo", "core")
    return jax.shard_map(
        shards,
        mesh=split_mesh,
        in_specs=(P("blk", dp), P("blk", dp), P(dp, "blk", None), P(dp, "blk", None)),
        out_specs=(P(dp, "blk", None), P(dp, "blk", None)),
        check_vma=False,
    )
```

```python
import math

import jax
import jax.numpy as jnp
from jax import lax
from jax.sharding import Mesh
from jax.sharding import PartitionSpec as P

NB = 1024
BS = 256


tanh_scale = 0.7978845608028654
cubic_coef = 0.044715


def gelu_value(values):
    inner = jnp.tanh(tanh_scale * (values + cubic_coef * values * values * values))
    return 0.5 * values * (1.0 + inner)


def gelu_slope(values):
    inner = jnp.tanh(tanh_scale * (values + cubic_coef * values * values * values))
    return 0.5 * (1.0 + inner) + 0.5 * values * (1.0 - inner * inner) * tanh_scale * (
        1.0 + 3.0 * cubic_coef * values * values
    )


def line_pairs(n, step):
    return [(i, i + step) for i in range(n) if 0 <= i + step < n]


def swap_pairs(n):
    return [(c, (c + 1) % n) for c in range(n)]


def gather_rows(piece):
    n_core = lax.axis_size("core")
    n_ylo = lax.axis_size("ylo")
    y = lax.axis_index("ylo")
    c = lax.axis_index("core")
    right = [piece]
    left = [piece]
    for _ in range(n_ylo - 1):
        right.append(lax.ppermute(right[-1], "ylo", line_pairs(n_ylo, 1)))
        left.append(lax.ppermute(left[-1], "ylo", line_pairs(n_ylo, -1)))
    stacked = jnp.stack(right[:0:-1] + left)
    line = lax.dynamic_slice_in_dim(stacked, n_ylo - 1 - y, n_ylo, axis=0)
    other = lax.ppermute(line, "core", swap_pairs(n_core))
    pair = jnp.where(c == 0, jnp.stack([line, other], 1), jnp.stack([other, line], 1))
    return pair.reshape((n_ylo * n_core * piece.shape[0],) + piece.shape[1:])


def scatter_rows(term):
    n_core = lax.axis_size("core")
    n_ylo = lax.axis_size("ylo")
    y = lax.axis_index("ylo")
    c = lax.axis_index("core")
    sent = lax.dynamic_index_in_dim(term, lax.rem(c + 1, n_core), 0, keepdims=False)
    kept = lax.dynamic_index_in_dim(term, c, 0, keepdims=False)
    got = lax.ppermute(sent, "core", swap_pairs(n_core))
    chip = kept.astype(jnp.float32) + got.astype(jnp.float32)
    total = lax.dynamic_index_in_dim(chip, y, 0, keepdims=False)
    for step in (1, -1):
        carry = None
        for s in range(1, n_ylo):
            dest = jnp.clip(y + step * (n_ylo - s), 0, n_ylo - 1)
            block = lax.dynamic_index_in_dim(chip, dest, 0, keepdims=False)
            if carry is not None:
                block = block + carry.astype(jnp.float32)
            carry = lax.ppermute(block.astype(jnp.bfloat16), "ylo", line_pairs(n_ylo, step))
        total = total + carry.astype(jnp.float32)
    return total.astype(jnp.bfloat16)


def shards(input_field, target_field, first_factor, second_factor):
    block_count = first_factor.shape[1]
    block_size = first_factor.shape[2]
    row_count = input_field.shape[1]
    replica_count = lax.axis_size("ylo") * lax.axis_size("core")
    group_count = NB // BS
    inner_count = block_count // group_count
    scale_factor = 1.0 / math.sqrt(row_count * replica_count)
    inputs = input_field.reshape(block_count, block_size, row_count)
    first_full = gather_rows(first_factor)
    second_full = lax.all_gather(second_factor, ("ylo", "core"), axis=0, tiled=True)
    pre_act = jnp.einsum("bkr,kbi->bir", inputs, first_full, preferred_element_type=jnp.float32)
    activated = gelu_value(pre_act).astype(jnp.bfloat16)
    received = lax.all_to_all(activated, "blk", split_axis=1, concat_axis=0, tiled=True)
    permuted = received.reshape(group_count, block_size, inner_count, row_count)
    targets = target_field.reshape(inner_count, group_count, block_size, row_count)
    count = second_full.shape[0]
    split_part = second_full.reshape(count, inner_count, group_count, block_size)
    predicted = jnp.einsum(
        "gcir,cigj->igjr", permuted, split_part, preferred_element_type=jnp.float32
    )
    residual = ((predicted - targets.astype(jnp.float32)) * scale_factor).astype(jnp.bfloat16)
    permuted_grad = jnp.einsum(
        "cigj,igjr->gcir", split_part, residual, preferred_element_type=jnp.float32
    ).astype(jnp.bfloat16)
    n_core = lax.axis_size("core")
    n_ylo = lax.axis_size("ylo")
    kk = block_size // (n_core * n_ylo)
    term = jnp.einsum(
        "gcir,igjr->cigj", permuted, residual, preferred_element_type=jnp.float32
    )
    second_out = lax.psum_scatter(
        term.reshape(count, block_count, block_size).astype(jnp.bfloat16),
        ("ylo", "core"),
        scatter_dimension=0,
        tiled=True,
    )
    sending = permuted_grad.reshape(group_count * block_size, inner_count, row_count)
    activated_grad = lax.all_to_all(sending, "blk", split_axis=0, concat_axis=1, tiled=True)
    pre_grad = (activated_grad.astype(jnp.float32) * gelu_slope(pre_act)).astype(jnp.bfloat16)
    inputs_cm = inputs.reshape(block_count, n_ylo, n_core, kk, row_count)
    first_sum = scatter_rows(
        jnp.einsum(
            "byxkr,bir->xykbi", inputs_cm, pre_grad, preferred_element_type=jnp.float32
        ).astype(jnp.bfloat16)
    )
    return (first_sum, second_out)


def solution(mesh):
    n_blk, n_dp = mesh.devices.shape
    n_core = 2
    split_mesh = Mesh(
        mesh.devices.reshape(n_blk, n_dp // n_core, n_core), ("blk", "ylo", "core")
    )
    dp = ("ylo", "core")
    return jax.shard_map(
        shards,
        mesh=split_mesh,
        in_specs=(P("blk", dp), P("blk", dp), P(dp, "blk", None), P(dp, "blk", None)),
        out_specs=(P(dp, "blk", None), P(dp, "blk", None)),
        check_vma=False,
    )
```

```python
import math

import jax
import jax.numpy as jnp
from jax import lax
from jax.sharding import Mesh
from jax.sharding import PartitionSpec as P

NB = 1024
BS = 256


tanh_scale = 0.7978845608028654
cubic_coef = 0.044715


def gelu_value(values):
    inner = jnp.tanh(tanh_scale * (values + cubic_coef * values * values * values))
    return 0.5 * values * (1.0 + inner)


def gelu_slope(values):
    inner = jnp.tanh(tanh_scale * (values + cubic_coef * values * values * values))
    return 0.5 * (1.0 + inner) + 0.5 * values * (1.0 - inner * inner) * tanh_scale * (
        1.0 + 3.0 * cubic_coef * values * values
    )


def line_pairs(n, step):
    return [(i, i + step) for i in range(n) if 0 <= i + step < n]


def swap_pairs(n):
    return [(c, (c + 1) % n) for c in range(n)]


def gather_rows(piece):
    n_core = lax.axis_size("core")
    n_ylo = lax.axis_size("ylo")
    y = lax.axis_index("ylo")
    c = lax.axis_index("core")
    right = [piece]
    left = [piece]
    for _ in range(n_ylo - 1):
        right.append(lax.ppermute(right[-1], "ylo", line_pairs(n_ylo, 1)))
        left.append(lax.ppermute(left[-1], "ylo", line_pairs(n_ylo, -1)))
    stacked = jnp.stack(right[:0:-1] + left)
    line = lax.dynamic_slice_in_dim(stacked, n_ylo - 1 - y, n_ylo, axis=0)
    other = lax.ppermute(line, "core", swap_pairs(n_core))
    pair = jnp.where(c == 0, jnp.stack([line, other], 1), jnp.stack([other, line], 1))
    return pair.reshape((n_ylo * n_core * piece.shape[0],) + piece.shape[1:])


def scatter_rows(term):
    n_core = lax.axis_size("core")
    n_ylo = lax.axis_size("ylo")
    y = lax.axis_index("ylo")
    c = lax.axis_index("core")
    sent = lax.dynamic_index_in_dim(term, lax.rem(c + 1, n_core), 0, keepdims=False)
    kept = lax.dynamic_index_in_dim(term, c, 0, keepdims=False)
    got = lax.ppermute(sent, "core", swap_pairs(n_core))
    chip = kept.astype(jnp.float32) + got.astype(jnp.float32)
    total = lax.dynamic_index_in_dim(chip, y, 0, keepdims=False)
    for step in (1, -1):
        carry = None
        for s in range(1, n_ylo):
            dest = jnp.clip(y + step * (n_ylo - s), 0, n_ylo - 1)
            block = lax.dynamic_index_in_dim(chip, dest, 0, keepdims=False)
            if carry is not None:
                block = block + carry.astype(jnp.float32)
            carry = lax.ppermute(block.astype(jnp.bfloat16), "ylo", line_pairs(n_ylo, step))
        total = total + carry.astype(jnp.float32)
    return total.astype(jnp.bfloat16)


def shards(input_field, target_field, first_factor, second_factor):
    block_count = first_factor.shape[1]
    block_size = first_factor.shape[2]
    row_count = input_field.shape[1]
    replica_count = lax.axis_size("ylo") * lax.axis_size("core")
    group_count = NB // BS
    inner_count = block_count // group_count
    scale_factor = 1.0 / math.sqrt(row_count * replica_count)
    inputs = input_field.reshape(block_count, block_size, row_count)
    both_full = gather_rows(jnp.stack([first_factor, second_factor], axis=1))
    first_full = both_full[:, 0]
    second_full = both_full[:, 1]
    pre_act = jnp.einsum("bkr,kbi->bir", inputs, first_full, preferred_element_type=jnp.float32)
    activated = gelu_value(pre_act).astype(jnp.bfloat16)
    received = lax.all_to_all(activated, "blk", split_axis=1, concat_axis=0, tiled=True)
    permuted = received.reshape(group_count, block_size, inner_count, row_count)
    targets = target_field.reshape(inner_count, group_count, block_size, row_count)
    count = second_full.shape[0]
    split_part = second_full.reshape(count, inner_count, group_count, block_size)
    predicted = jnp.einsum(
        "gcir,cigj->igjr", permuted, split_part, preferred_element_type=jnp.float32
    )
    residual = ((predicted - targets.astype(jnp.float32)) * scale_factor).astype(jnp.bfloat16)
    permuted_grad = jnp.einsum(
        "cigj,igjr->gcir", split_part, residual, preferred_element_type=jnp.float32
    ).astype(jnp.bfloat16)
    n_core = lax.axis_size("core")
    n_ylo = lax.axis_size("ylo")
    kk = block_size // (n_core * n_ylo)
    term = jnp.einsum(
        "gcir,igjr->cigj", permuted, residual, preferred_element_type=jnp.float32
    )
    second_out = lax.psum_scatter(
        term.reshape(count, block_count, block_size).astype(jnp.bfloat16),
        ("ylo", "core"),
        scatter_dimension=0,
        tiled=True,
    )
    sending = permuted_grad.reshape(group_count * block_size, inner_count, row_count)
    activated_grad = lax.all_to_all(sending, "blk", split_axis=0, concat_axis=1, tiled=True)
    pre_grad = (activated_grad.astype(jnp.float32) * gelu_slope(pre_act)).astype(jnp.bfloat16)
    inputs_cm = inputs.reshape(block_count, n_ylo, n_core, kk, row_count)
    first_sum = scatter_rows(
        jnp.einsum(
            "byxkr,bir->xykbi", inputs_cm, pre_grad, preferred_element_type=jnp.float32
        ).astype(jnp.bfloat16)
    )
    return (first_sum, second_out)


def solution(mesh):
    n_blk, n_dp = mesh.devices.shape
    n_core = 2
    split_mesh = Mesh(
        mesh.devices.reshape(n_blk, n_dp // n_core, n_core), ("blk", "ylo", "core")
    )
    dp = ("ylo", "core")
    return jax.shard_map(
        shards,
        mesh=split_mesh,
        in_specs=(P("blk", dp), P("blk", dp), P(dp, "blk", None), P(dp, "blk", None)),
        out_specs=(P(dp, "blk", None), P(dp, "blk", None)),
        check_vma=False,
    )
```

```python
import math

import jax
import jax.numpy as jnp
from jax import lax
from jax.sharding import Mesh
from jax.sharding import PartitionSpec as P

NB = 1024
BS = 256


tanh_scale = 0.7978845608028654
cubic_coef = 0.044715


def gelu_value(values):
    inner = jnp.tanh(tanh_scale * (values + cubic_coef * values * values * values))
    return 0.5 * values * (1.0 + inner)


def gelu_slope(values):
    inner = jnp.tanh(tanh_scale * (values + cubic_coef * values * values * values))
    return 0.5 * (1.0 + inner) + 0.5 * values * (1.0 - inner * inner) * tanh_scale * (
        1.0 + 3.0 * cubic_coef * values * values
    )


def line_pairs(n, step):
    return [(i, i + step) for i in range(n) if 0 <= i + step < n]


def swap_pairs(n):
    return [(c, (c + 1) % n) for c in range(n)]


def gather_rows(piece):
    n_core = lax.axis_size("core")
    n_ylo = lax.axis_size("ylo")
    y = lax.axis_index("ylo")
    c = lax.axis_index("core")
    right = [piece]
    left = [piece]
    for _ in range(n_ylo - 1):
        right.append(lax.ppermute(right[-1], "ylo", line_pairs(n_ylo, 1)))
        left.append(lax.ppermute(left[-1], "ylo", line_pairs(n_ylo, -1)))
    stacked = jnp.stack(right[:0:-1] + left)
    line = lax.dynamic_slice_in_dim(stacked, n_ylo - 1 - y, n_ylo, axis=0)
    other = lax.ppermute(line, "core", swap_pairs(n_core))
    pair = jnp.where(c == 0, jnp.stack([line, other], 1), jnp.stack([other, line], 1))
    return pair.reshape((n_ylo * n_core * piece.shape[0],) + piece.shape[1:])


def scatter_rows(term):
    n_core = lax.axis_size("core")
    n_ylo = lax.axis_size("ylo")
    y = lax.axis_index("ylo")
    c = lax.axis_index("core")
    sent = lax.dynamic_index_in_dim(term, lax.rem(c + 1, n_core), 0, keepdims=False)
    kept = lax.dynamic_index_in_dim(term, c, 0, keepdims=False)
    got = lax.ppermute(sent, "core", swap_pairs(n_core))
    chip = kept.astype(jnp.float32) + got.astype(jnp.float32)
    total = lax.dynamic_index_in_dim(chip, y, 0, keepdims=False)
    for step in (1, -1):
        carry = None
        for s in range(1, n_ylo):
            dest = jnp.clip(y + step * (n_ylo - s), 0, n_ylo - 1)
            block = lax.dynamic_index_in_dim(chip, dest, 0, keepdims=False)
            if carry is not None:
                block = block + carry.astype(jnp.float32)
            carry = lax.ppermute(block.astype(jnp.bfloat16), "ylo", line_pairs(n_ylo, step))
        total = total + carry.astype(jnp.float32)
    return total.astype(jnp.bfloat16)


def shards(input_field, target_field, first_factor, second_factor):
    block_count = first_factor.shape[1]
    block_size = first_factor.shape[2]
    row_count = input_field.shape[1]
    dp = ("ylo", "core")
    replica_count = lax.axis_size("ylo") * lax.axis_size("core")
    blk_count = lax.axis_size("blk")
    group_count = NB // BS
    inner_count = block_count // group_count
    scale_factor = 1.0 / math.sqrt(row_count * replica_count)
    inputs = input_field.reshape(block_count, block_size, row_count)
    first_full = gather_rows(first_factor)
    second_full = lax.all_gather(second_factor, dp, axis=0, tiled=True)
    pre_act = jnp.einsum("bkr,kbi->bir", inputs, first_full, preferred_element_type=jnp.float32)
    pre_split = pre_act.reshape(block_count, blk_count, inner_count, row_count)
    activated = gelu_value(pre_split).astype(jnp.bfloat16)
    slope = jnp.transpose(gelu_slope(pre_split), (2, 1, 0, 3))
    sending = jnp.transpose(activated, (2, 1, 0, 3))
    received = lax.all_to_all(sending, "blk", split_axis=1, concat_axis=1, tiled=True)
    permuted = received.reshape(block_count, block_size, row_count)
    targets = target_field.reshape(block_count, block_size, row_count)
    second_t = jnp.transpose(second_full, (1, 0, 2))
    predicted = jnp.einsum(
        "qcj,qcr->qjr", second_t, permuted, preferred_element_type=jnp.float32
    )
    residual = ((predicted - targets.astype(jnp.float32)) * scale_factor).astype(jnp.bfloat16)
    permuted_grad = jnp.einsum(
        "qcj,qjr->qcr", second_t, residual, preferred_element_type=jnp.float32
    ).astype(jnp.bfloat16)
    term = jnp.einsum("qcr,qjr->cqj", permuted, residual, preferred_element_type=jnp.float32)
    second_out = lax.psum_scatter(
        term.astype(jnp.bfloat16), dp, scatter_dimension=0, tiled=True
    )
    back = permuted_grad.reshape(inner_count, blk_count, block_count, row_count)
    activated_grad = lax.all_to_all(back, "blk", split_axis=1, concat_axis=1, tiled=True)
    pre_grad = (activated_grad.astype(jnp.float32) * slope).astype(jnp.bfloat16)
    pre_grad = jnp.transpose(pre_grad, (2, 1, 0, 3)).reshape(block_count, block_size, row_count)
    first_sum = lax.psum_scatter(
        jnp.einsum("bkr,bir->kbi", inputs, pre_grad, preferred_element_type=jnp.float32).astype(
            jnp.bfloat16
        ),
        dp,
        scatter_dimension=0,
        tiled=True,
    )
    return (first_sum, second_out)


def solution(mesh):
    n_blk, n_dp = mesh.devices.shape
    n_core = 2
    split_mesh = Mesh(
        mesh.devices.reshape(n_blk, n_dp // n_core, n_core), ("blk", "ylo", "core")
    )
    dp = ("ylo", "core")
    return jax.shard_map(
        shards,
        mesh=split_mesh,
        in_specs=(P("blk", dp), P("blk", dp), P(dp, "blk", None), P(dp, "blk", None)),
        out_specs=(P(dp, "blk", None), P(dp, "blk", None)),
        check_vma=False,
    )
```

```python
import math

import jax
import jax.numpy as jnp
from jax import lax
from jax.sharding import Mesh
from jax.sharding import PartitionSpec as P

NB = 1024
BS = 256


tanh_scale = 0.7978845608028654
cubic_coef = 0.044715


def gelu_value(values):
    inner = jnp.tanh(tanh_scale * (values + cubic_coef * values * values * values))
    return 0.5 * values * (1.0 + inner)


def gelu_slope(values):
    inner = jnp.tanh(tanh_scale * (values + cubic_coef * values * values * values))
    return 0.5 * (1.0 + inner) + 0.5 * values * (1.0 - inner * inner) * tanh_scale * (
        1.0 + 3.0 * cubic_coef * values * values
    )


def line_pairs(n, step):
    return [(i, i + step) for i in range(n) if 0 <= i + step < n]


def swap_pairs(n):
    return [(c, (c + 1) % n) for c in range(n)]


def swap_pairs(n):
    return [(c, (c + 1) % n) for c in range(n)]


def gather_rows(piece):
    n_core = lax.axis_size("core")
    n_ylo = lax.axis_size("ylo")
    c = lax.axis_index("core")
    copies = jnp.broadcast_to(piece[None], (n_ylo,) + piece.shape)
    line = lax.all_to_all(copies, "ylo", split_axis=0, concat_axis=0, tiled=True)
    other = lax.ppermute(line, "core", swap_pairs(n_core))
    pair = jnp.where(c == 0, jnp.stack([line, other], 1), jnp.stack([other, line], 1))
    return pair.reshape((n_ylo * n_core * piece.shape[0],) + piece.shape[1:])


def scatter_rows(term):
    n_core = lax.axis_size("core")
    n_ylo = lax.axis_size("ylo")
    c = lax.axis_index("core")
    blocks, total_rows, width = term.shape
    rows = total_rows // (n_core * n_ylo)
    split = term.reshape(blocks, n_ylo, n_core, rows, width)
    sent = lax.dynamic_index_in_dim(split, lax.rem(c + 1, n_core), 2, keepdims=False)
    kept = lax.dynamic_index_in_dim(split, c, 2, keepdims=False)
    got = lax.ppermute(sent, "core", swap_pairs(n_core))
    half = (kept.astype(jnp.float32) + got.astype(jnp.float32)).astype(jnp.bfloat16)
    arrived = lax.all_to_all(half, "ylo", split_axis=1, concat_axis=1, tiled=True)
    total = jnp.sum(arrived.astype(jnp.float32), axis=1).astype(jnp.bfloat16)
    return jnp.transpose(total, (1, 0, 2))


def shards(input_field, target_field, first_factor, second_factor):
    block_count = first_factor.shape[1]
    block_size = first_factor.shape[2]
    row_count = input_field.shape[1]
    dp = ("ylo", "core")
    replica_count = lax.axis_size("ylo") * lax.axis_size("core")
    blk_count = lax.axis_size("blk")
    group_count = NB // BS
    inner_count = block_count // group_count
    scale_factor = 1.0 / math.sqrt(row_count * replica_count)
    inputs = input_field.reshape(block_count, block_size, row_count)
    first_full = gather_rows(first_factor)
    second_full = lax.all_gather(second_factor, dp, axis=0, tiled=True)
    pre_act = jnp.einsum("bkr,kbi->bir", inputs, first_full, preferred_element_type=jnp.float32)
    pre_split = pre_act.reshape(block_count, blk_count, inner_count, row_count)
    activated = gelu_value(pre_split).astype(jnp.bfloat16)
    slope = jnp.transpose(gelu_slope(pre_split), (2, 1, 0, 3))
    sending = jnp.transpose(activated, (2, 1, 0, 3))
    received = lax.all_to_all(sending, "blk", split_axis=1, concat_axis=1, tiled=True)
    permuted = received.reshape(block_count, block_size, row_count)
    targets = target_field.reshape(block_count, block_size, row_count)
    second_t = jnp.transpose(second_full, (1, 0, 2))
    predicted = jnp.einsum(
        "qcj,qcr->qjr", second_t, permuted, preferred_element_type=jnp.float32
    )
    residual = ((predicted - targets.astype(jnp.float32)) * scale_factor).astype(jnp.bfloat16)
    permuted_grad = jnp.einsum(
        "qcj,qjr->qcr", second_t, residual, preferred_element_type=jnp.float32
    ).astype(jnp.bfloat16)
    term = jnp.einsum("qcr,qjr->cqj", permuted, residual, preferred_element_type=jnp.float32)
    second_out = lax.psum_scatter(
        term.astype(jnp.bfloat16), dp, scatter_dimension=0, tiled=True
    )
    back = permuted_grad.reshape(inner_count, blk_count, block_count, row_count)
    activated_grad = lax.all_to_all(back, "blk", split_axis=1, concat_axis=1, tiled=True)
    pre_grad = (activated_grad.astype(jnp.float32) * slope).astype(jnp.bfloat16)
    pre_grad = jnp.transpose(pre_grad, (2, 1, 0, 3)).reshape(block_count, block_size, row_count)
    first_sum = scatter_rows(
        jnp.einsum("bkr,bir->bki", inputs, pre_grad, preferred_element_type=jnp.float32).astype(
            jnp.bfloat16
        )
    )
    return (first_sum, second_out)


def solution(mesh):
    n_blk, n_dp = mesh.devices.shape
    n_core = 2
    split_mesh = Mesh(
        mesh.devices.reshape(n_blk, n_dp // n_core, n_core), ("blk", "ylo", "core")
    )
    dp = ("ylo", "core")
    return jax.shard_map(
        shards,
        mesh=split_mesh,
        in_specs=(P("blk", dp), P("blk", dp), P(dp, "blk", None), P(dp, "blk", None)),
        out_specs=(P(dp, "blk", None), P(dp, "blk", None)),
        check_vma=False,
    )
```

```python
import math

import jax
import jax.numpy as jnp
from jax import lax
from jax.sharding import Mesh
from jax.sharding import PartitionSpec as P

NB = 1024
BS = 256


tanh_scale = 0.7978845608028654
cubic_coef = 0.044715


def gelu_value(values):
    inner = jnp.tanh(tanh_scale * (values + cubic_coef * values * values * values))
    return 0.5 * values * (1.0 + inner)


def gelu_slope(values):
    inner = jnp.tanh(tanh_scale * (values + cubic_coef * values * values * values))
    return 0.5 * (1.0 + inner) + 0.5 * values * (1.0 - inner * inner) * tanh_scale * (
        1.0 + 3.0 * cubic_coef * values * values
    )


def line_pairs(n, step):
    return [(i, i + step) for i in range(n) if 0 <= i + step < n]


def swap_pairs(n):
    return [(c, (c + 1) % n) for c in range(n)]


def swap_pairs(n):
    return [(c, (c + 1) % n) for c in range(n)]


def gather_rows(piece):
    n_core = lax.axis_size("core")
    n_ylo = lax.axis_size("ylo")
    c = lax.axis_index("core")
    copies = jnp.broadcast_to(piece[None], (n_ylo,) + piece.shape)
    line = lax.all_to_all(copies, "ylo", split_axis=0, concat_axis=0, tiled=True)
    other = lax.ppermute(line, "core", swap_pairs(n_core))
    pair = jnp.where(c == 0, jnp.stack([line, other], 1), jnp.stack([other, line], 1))
    return pair.reshape((n_ylo * n_core * piece.shape[0],) + piece.shape[1:])


def scatter_rows(term):
    n_core = lax.axis_size("core")
    n_ylo = lax.axis_size("ylo")
    c = lax.axis_index("core")
    blocks, total_rows, width = term.shape
    rows = total_rows // (n_core * n_ylo)
    split = term.reshape(blocks, n_ylo, n_core, rows, width)
    sent = lax.dynamic_index_in_dim(split, lax.rem(c + 1, n_core), 2, keepdims=False)
    kept = lax.dynamic_index_in_dim(split, c, 2, keepdims=False)
    got = lax.ppermute(sent, "core", swap_pairs(n_core))
    half = (kept.astype(jnp.float32) + got.astype(jnp.float32)).astype(jnp.bfloat16)
    arrived = lax.all_to_all(half, "ylo", split_axis=1, concat_axis=1, tiled=True)
    total = jnp.sum(arrived.astype(jnp.float32), axis=1).astype(jnp.bfloat16)
    return jnp.transpose(total, (1, 0, 2))


def shards(input_field, target_field, first_factor, second_factor):
    block_count = first_factor.shape[1]
    block_size = first_factor.shape[2]
    row_count = input_field.shape[1]
    dp = ("ylo", "core")
    replica_count = lax.axis_size("ylo") * lax.axis_size("core")
    blk_count = lax.axis_size("blk")
    group_count = NB // BS
    inner_count = block_count // group_count
    scale_factor = 1.0 / math.sqrt(row_count * replica_count)
    inputs = input_field.reshape(block_count, block_size, row_count)
    first_full = gather_rows(first_factor)
    second_full = lax.all_gather(second_factor, dp, axis=0, tiled=True)
    pre_act = jnp.einsum("bkr,kbi->bir", inputs, first_full, preferred_element_type=jnp.float32)
    pre_split = pre_act.reshape(block_count, blk_count, inner_count, row_count)
    activated = gelu_value(pre_split).astype(jnp.bfloat16)
    slope = jnp.transpose(gelu_slope(pre_split).astype(jnp.bfloat16), (2, 1, 0, 3))
    sending = jnp.transpose(activated, (2, 1, 0, 3))
    received = lax.all_to_all(sending, "blk", split_axis=1, concat_axis=1, tiled=True)
    permuted = received.reshape(block_count, block_size, row_count)
    targets = target_field.reshape(block_count, block_size, row_count)
    second_t = jnp.transpose(second_full, (1, 0, 2))
    predicted = jnp.einsum(
        "qcj,qcr->qjr", second_t, permuted, preferred_element_type=jnp.float32
    )
    residual = ((predicted - targets.astype(jnp.float32)) * scale_factor).astype(jnp.bfloat16)
    permuted_grad = jnp.einsum(
        "qcj,qjr->qcr", second_t, residual, preferred_element_type=jnp.float32
    ).astype(jnp.bfloat16)
    term = jnp.einsum("qcr,qjr->cqj", permuted, residual, preferred_element_type=jnp.float32)
    second_out = lax.psum_scatter(
        term.astype(jnp.bfloat16), dp, scatter_dimension=0, tiled=True
    )
    back = permuted_grad.reshape(inner_count, blk_count, block_count, row_count)
    activated_grad = lax.all_to_all(back, "blk", split_axis=1, concat_axis=1, tiled=True)
    pre_grad = (activated_grad.astype(jnp.float32) * slope).astype(jnp.bfloat16)
    pre_grad = jnp.transpose(pre_grad, (2, 1, 0, 3)).reshape(block_count, block_size, row_count)
    first_sum = scatter_rows(
        jnp.einsum("bkr,bir->bki", inputs, pre_grad, preferred_element_type=jnp.float32).astype(
            jnp.bfloat16
        )
    )
    return (first_sum, second_out)


def solution(mesh):
    n_blk, n_dp = mesh.devices.shape
    n_core = 2
    split_mesh = Mesh(
        mesh.devices.reshape(n_blk, n_dp // n_core, n_core), ("blk", "ylo", "core")
    )
    dp = ("ylo", "core")
    return jax.shard_map(
        shards,
        mesh=split_mesh,
        in_specs=(P("blk", dp), P("blk", dp), P(dp, "blk", None), P(dp, "blk", None)),
        out_specs=(P(dp, "blk", None), P(dp, "blk", None)),
        check_vma=False,
    )
```

```python
import math

import jax
import jax.numpy as jnp
from jax import lax
from jax.sharding import Mesh
from jax.sharding import PartitionSpec as P

NB = 1024
BS = 256


tanh_scale = 0.7978845608028654
cubic_coef = 0.044715


def gelu_value(values):
    inner = jnp.tanh(tanh_scale * (values + cubic_coef * values * values * values))
    return 0.5 * values * (1.0 + inner)


def gelu_slope(values):
    inner = jnp.tanh(tanh_scale * (values + cubic_coef * values * values * values))
    return 0.5 * (1.0 + inner) + 0.5 * values * (1.0 - inner * inner) * tanh_scale * (
        1.0 + 3.0 * cubic_coef * values * values
    )


def line_pairs(n, step):
    return [(i, i + step) for i in range(n) if 0 <= i + step < n]


def swap_pairs(n):
    return [(c, (c + 1) % n) for c in range(n)]


def swap_pairs(n):
    return [(c, (c + 1) % n) for c in range(n)]


def gather_rows(piece):
    n_core = lax.axis_size("core")
    n_ylo = lax.axis_size("ylo")
    c = lax.axis_index("core")
    copies = jnp.broadcast_to(piece[None], (n_ylo,) + piece.shape)
    line = lax.all_to_all(copies, "ylo", split_axis=0, concat_axis=0, tiled=True)
    other = lax.ppermute(line, "core", swap_pairs(n_core))
    pair = jnp.where(c == 0, jnp.stack([line, other], 1), jnp.stack([other, line], 1))
    return pair.reshape((n_ylo * n_core * piece.shape[0],) + piece.shape[1:])


def scatter_rows(term):
    n_core = lax.axis_size("core")
    n_ylo = lax.axis_size("ylo")
    c = lax.axis_index("core")
    blocks, total_rows, width = term.shape
    rows = total_rows // (n_core * n_ylo)
    split = term.reshape(blocks, n_ylo, n_core, rows, width)
    sent = lax.dynamic_index_in_dim(split, lax.rem(c + 1, n_core), 2, keepdims=False)
    kept = lax.dynamic_index_in_dim(split, c, 2, keepdims=False)
    got = lax.ppermute(sent, "core", swap_pairs(n_core))
    half = (kept.astype(jnp.float32) + got.astype(jnp.float32)).astype(jnp.bfloat16)
    arrived = lax.all_to_all(half, "ylo", split_axis=1, concat_axis=1, tiled=True)
    total = jnp.sum(arrived.astype(jnp.float32), axis=1).astype(jnp.bfloat16)
    return jnp.transpose(total, (1, 0, 2))


def shards(input_field, target_field, first_factor, second_factor):
    block_count = first_factor.shape[1]
    block_size = first_factor.shape[2]
    row_count = input_field.shape[1]
    dp = ("ylo", "core")
    replica_count = lax.axis_size("ylo") * lax.axis_size("core")
    blk_count = lax.axis_size("blk")
    group_count = NB // BS
    inner_count = block_count // group_count
    scale_factor = 1.0 / math.sqrt(row_count * replica_count)
    inputs = input_field.reshape(block_count, block_size, row_count)
    first_full = gather_rows(first_factor)
    second_full = lax.all_gather(second_factor, dp, axis=0, tiled=True)
    pre_act = jnp.einsum("bkr,kbi->bir", inputs, first_full, preferred_element_type=jnp.float32)
    pre_split = pre_act.reshape(block_count, blk_count, inner_count, row_count)
    activated = gelu_value(pre_split).astype(jnp.bfloat16)
    slope = jnp.transpose(gelu_slope(pre_split), (2, 1, 0, 3))
    activated, second_full = lax.optimization_barrier((activated, second_full))
    sending = jnp.transpose(activated, (2, 1, 0, 3))
    received = lax.all_to_all(sending, "blk", split_axis=1, concat_axis=1, tiled=True)
    permuted = received.reshape(block_count, block_size, row_count)
    targets = target_field.reshape(block_count, block_size, row_count)
    second_t = jnp.transpose(second_full, (1, 0, 2))
    predicted = jnp.einsum(
        "qcj,qcr->qjr", second_t, permuted, preferred_element_type=jnp.float32
    )
    residual = ((predicted - targets.astype(jnp.float32)) * scale_factor).astype(jnp.bfloat16)
    permuted_grad = jnp.einsum(
        "qcj,qjr->qcr", second_t, residual, preferred_element_type=jnp.float32
    ).astype(jnp.bfloat16)
    term = jnp.einsum("qcr,qjr->cqj", permuted, residual, preferred_element_type=jnp.float32)
    second_out = lax.psum_scatter(
        term.astype(jnp.bfloat16), dp, scatter_dimension=0, tiled=True
    )
    back = permuted_grad.reshape(inner_count, blk_count, block_count, row_count)
    activated_grad = lax.all_to_all(back, "blk", split_axis=1, concat_axis=1, tiled=True)
    pre_grad = (activated_grad.astype(jnp.float32) * slope).astype(jnp.bfloat16)
    pre_grad = jnp.transpose(pre_grad, (2, 1, 0, 3)).reshape(block_count, block_size, row_count)
    first_sum = scatter_rows(
        jnp.einsum("bkr,bir->bki", inputs, pre_grad, preferred_element_type=jnp.float32).astype(
            jnp.bfloat16
        )
    )
    return (first_sum, second_out)


def solution(mesh):
    n_blk, n_dp = mesh.devices.shape
    n_core = 2
    split_mesh = Mesh(
        mesh.devices.reshape(n_blk, n_dp // n_core, n_core), ("blk", "ylo", "core")
    )
    dp = ("ylo", "core")
    return jax.shard_map(
        shards,
        mesh=split_mesh,
        in_specs=(P("blk", dp), P("blk", dp), P(dp, "blk", None), P(dp, "blk", None)),
        out_specs=(P(dp, "blk", None), P(dp, "blk", None)),
        check_vma=False,
    )
```

```python
import math

import jax
import jax.numpy as jnp
from jax import lax
from jax.sharding import Mesh
from jax.sharding import PartitionSpec as P

NB = 1024
BS = 256


tanh_scale = 0.7978845608028654
cubic_coef = 0.044715


def gelu_value(values):
    inner = jnp.tanh(tanh_scale * (values + cubic_coef * values * values * values))
    return 0.5 * values * (1.0 + inner)


def gelu_slope(values):
    inner = jnp.tanh(tanh_scale * (values + cubic_coef * values * values * values))
    return 0.5 * (1.0 + inner) + 0.5 * values * (1.0 - inner * inner) * tanh_scale * (
        1.0 + 3.0 * cubic_coef * values * values
    )


def line_pairs(n, step):
    return [(i, i + step) for i in range(n) if 0 <= i + step < n]


def swap_pairs(n):
    return [(c, (c + 1) % n) for c in range(n)]


def swap_pairs(n):
    return [(c, (c + 1) % n) for c in range(n)]


def gather_rows(piece):
    n_core = lax.axis_size("core")
    n_ylo = lax.axis_size("ylo")
    c = lax.axis_index("core")
    copies = jnp.broadcast_to(piece[None], (n_ylo,) + piece.shape)
    line = lax.all_to_all(copies, "ylo", split_axis=0, concat_axis=0, tiled=True)
    other = lax.ppermute(line, "core", swap_pairs(n_core))
    pair = jnp.zeros((n_ylo, n_core) + piece.shape, piece.dtype)
    pair = lax.dynamic_update_index_in_dim(pair, line, c, 1)
    pair = lax.dynamic_update_index_in_dim(pair, other, lax.rem(c + 1, n_core), 1)
    return pair.reshape((n_ylo * n_core * piece.shape[0],) + piece.shape[1:])


def scatter_rows(term):
    n_core = lax.axis_size("core")
    n_ylo = lax.axis_size("ylo")
    c = lax.axis_index("core")
    blocks, total_rows, width = term.shape
    rows = total_rows // (n_core * n_ylo)
    split = term.reshape(blocks, n_ylo, n_core, rows, width)
    sent = lax.dynamic_index_in_dim(split, lax.rem(c + 1, n_core), 2, keepdims=False)
    kept = lax.dynamic_index_in_dim(split, c, 2, keepdims=False)
    got = lax.ppermute(sent, "core", swap_pairs(n_core))
    half = (kept.astype(jnp.float32) + got.astype(jnp.float32)).astype(jnp.bfloat16)
    arrived = lax.all_to_all(half, "ylo", split_axis=1, concat_axis=1, tiled=True)
    total = jnp.sum(arrived.astype(jnp.float32), axis=1).astype(jnp.bfloat16)
    return jnp.transpose(total, (1, 0, 2))


def shards(input_field, target_field, first_factor, second_factor):
    block_count = first_factor.shape[1]
    block_size = first_factor.shape[2]
    row_count = input_field.shape[1]
    dp = ("ylo", "core")
    replica_count = lax.axis_size("ylo") * lax.axis_size("core")
    blk_count = lax.axis_size("blk")
    group_count = NB // BS
    inner_count = block_count // group_count
    scale_factor = 1.0 / math.sqrt(row_count * replica_count)
    inputs = input_field.reshape(block_count, block_size, row_count)
    first_full = gather_rows(first_factor)
    second_full = lax.all_gather(second_factor, dp, axis=0, tiled=True)
    pre_act = jnp.einsum("bkr,kbi->bir", inputs, first_full, preferred_element_type=jnp.float32)
    pre_split = pre_act.reshape(block_count, blk_count, inner_count, row_count)
    activated = gelu_value(pre_split).astype(jnp.bfloat16)
    slope = jnp.transpose(gelu_slope(pre_split).astype(jnp.bfloat16), (2, 1, 0, 3))
    activated, second_full, slope = lax.optimization_barrier((activated, second_full, slope))
    sending = jnp.transpose(activated, (2, 1, 0, 3))
    received = lax.all_to_all(sending, "blk", split_axis=1, concat_axis=1, tiled=True)
    permuted = received.reshape(block_count, block_size, row_count)
    targets = target_field.reshape(block_count, block_size, row_count)
    second_t = jnp.transpose(second_full, (1, 0, 2))
    predicted = jnp.einsum(
        "qcj,qcr->qjr", second_t, permuted, preferred_element_type=jnp.float32
    )
    residual = ((predicted - targets.astype(jnp.float32)) * scale_factor).astype(jnp.bfloat16)
    permuted_grad = jnp.einsum(
        "qcj,qjr->qcr", second_t, residual, preferred_element_type=jnp.float32
    ).astype(jnp.bfloat16)
    term = jnp.einsum("qcr,qjr->cqj", permuted, residual, preferred_element_type=jnp.float32)
    second_out = lax.psum_scatter(
        term.astype(jnp.bfloat16), dp, scatter_dimension=0, tiled=True
    )
    back = permuted_grad.reshape(inner_count, blk_count, block_count, row_count)
    activated_grad = lax.all_to_all(back, "blk", split_axis=1, concat_axis=1, tiled=True)
    pre_grad = (activated_grad.astype(jnp.float32) * slope).astype(jnp.bfloat16)
    pre_grad = jnp.transpose(pre_grad, (2, 1, 0, 3)).reshape(block_count, block_size, row_count)
    first_sum = scatter_rows(
        jnp.einsum("bkr,bir->bki", inputs, pre_grad, preferred_element_type=jnp.float32).astype(
            jnp.bfloat16
        )
    )
    return (first_sum, second_out)


def solution(mesh):
    n_blk, n_dp = mesh.devices.shape
    n_core = 2
    split_mesh = Mesh(
        mesh.devices.reshape(n_blk, n_dp // n_core, n_core), ("blk", "ylo", "core")
    )
    dp = ("ylo", "core")
    return jax.shard_map(
        shards,
        mesh=split_mesh,
        in_specs=(P("blk", dp), P("blk", dp), P(dp, "blk", None), P(dp, "blk", None)),
        out_specs=(P(dp, "blk", None), P(dp, "blk", None)),
        check_vma=False,
    )
```

```python
import math

import jax
import jax.numpy as jnp
from jax import lax
from jax.experimental.layout import Layout, with_layout_constraint
from jax.sharding import Mesh
from jax.sharding import PartitionSpec as P

NB = 1024
BS = 256


tanh_scale = 0.7978845608028654
cubic_coef = 0.044715


def gelu_value(values):
    inner = jnp.tanh(tanh_scale * (values + cubic_coef * values * values * values))
    return 0.5 * values * (1.0 + inner)


def gelu_slope(values):
    inner = jnp.tanh(tanh_scale * (values + cubic_coef * values * values * values))
    return 0.5 * (1.0 + inner) + 0.5 * values * (1.0 - inner * inner) * tanh_scale * (
        1.0 + 3.0 * cubic_coef * values * values
    )


def line_pairs(n, step):
    return [(i, i + step) for i in range(n) if 0 <= i + step < n]


def swap_pairs(n):
    return [(c, (c + 1) % n) for c in range(n)]


def swap_pairs(n):
    return [(c, (c + 1) % n) for c in range(n)]


def gather_rows(piece):
    n_core = lax.axis_size("core")
    n_ylo = lax.axis_size("ylo")
    c = lax.axis_index("core")
    copies = jnp.broadcast_to(piece[None], (n_ylo,) + piece.shape)
    line = lax.all_to_all(copies, "ylo", split_axis=0, concat_axis=0, tiled=True)
    other = lax.ppermute(line, "core", swap_pairs(n_core))
    pair = jnp.zeros((n_ylo, n_core) + piece.shape, piece.dtype)
    pair = lax.dynamic_update_index_in_dim(pair, line, c, 1)
    pair = lax.dynamic_update_index_in_dim(pair, other, lax.rem(c + 1, n_core), 1)
    return pair.reshape((n_ylo * n_core * piece.shape[0],) + piece.shape[1:])


def scatter_rows(term):
    n_core = lax.axis_size("core")
    n_ylo = lax.axis_size("ylo")
    c = lax.axis_index("core")
    blocks, total_rows, width = term.shape
    rows = total_rows // (n_core * n_ylo)
    split = term.reshape(blocks, n_ylo, n_core, rows, width)
    sent = lax.dynamic_index_in_dim(split, lax.rem(c + 1, n_core), 2, keepdims=False)
    kept = lax.dynamic_index_in_dim(split, c, 2, keepdims=False)
    got = lax.ppermute(sent, "core", swap_pairs(n_core))
    half = (kept.astype(jnp.float32) + got.astype(jnp.float32)).astype(jnp.bfloat16)
    arrived = lax.all_to_all(half, "ylo", split_axis=1, concat_axis=1, tiled=True)
    total = jnp.sum(arrived.astype(jnp.float32), axis=1).astype(jnp.bfloat16)
    return jnp.transpose(total, (1, 0, 2))


def shards(input_field, target_field, first_factor, second_factor):
    block_count = first_factor.shape[1]
    block_size = first_factor.shape[2]
    row_count = input_field.shape[1]
    dp = ("ylo", "core")
    replica_count = lax.axis_size("ylo") * lax.axis_size("core")
    blk_count = lax.axis_size("blk")
    group_count = NB // BS
    inner_count = block_count // group_count
    scale_factor = 1.0 / math.sqrt(row_count * replica_count)
    inputs = input_field.reshape(block_count, block_size, row_count)
    first_full = gather_rows(first_factor)
    second_full = lax.all_gather(second_factor, dp, axis=0, tiled=True)
    pre_act = jnp.einsum("bkr,kbi->bir", inputs, first_full, preferred_element_type=jnp.float32)
    pre_split = pre_act.reshape(block_count, blk_count, inner_count, row_count)
    activated = gelu_value(pre_split).astype(jnp.bfloat16)
    slope = jnp.transpose(gelu_slope(pre_split).astype(jnp.bfloat16), (2, 1, 0, 3))
    activated, second_full, slope = lax.optimization_barrier((activated, second_full, slope))
    sending = jnp.transpose(activated, (2, 1, 0, 3))
    sending = with_layout_constraint(sending, Layout((1, 0, 2, 3)))
    received = lax.all_to_all(sending, "blk", split_axis=1, concat_axis=1, tiled=True)
    permuted = received.reshape(block_count, block_size, row_count)
    targets = target_field.reshape(block_count, block_size, row_count)
    second_t = jnp.transpose(second_full, (1, 0, 2))
    predicted = jnp.einsum(
        "qcj,qcr->qjr", second_t, permuted, preferred_element_type=jnp.float32
    )
    residual = ((predicted - targets.astype(jnp.float32)) * scale_factor).astype(jnp.bfloat16)
    permuted_grad = jnp.einsum(
        "qcj,qjr->qcr", second_t, residual, preferred_element_type=jnp.float32
    ).astype(jnp.bfloat16)
    term = jnp.einsum("qcr,qjr->cqj", permuted, residual, preferred_element_type=jnp.float32)
    second_out = lax.psum_scatter(
        term.astype(jnp.bfloat16), dp, scatter_dimension=0, tiled=True
    )
    back = permuted_grad.reshape(inner_count, blk_count, block_count, row_count)
    back = with_layout_constraint(back, Layout((1, 0, 2, 3)))
    activated_grad = lax.all_to_all(back, "blk", split_axis=1, concat_axis=1, tiled=True)
    pre_grad = (activated_grad.astype(jnp.float32) * slope).astype(jnp.bfloat16)
    pre_grad = jnp.transpose(pre_grad, (2, 1, 0, 3)).reshape(block_count, block_size, row_count)
    first_sum = scatter_rows(
        jnp.einsum("bkr,bir->bki", inputs, pre_grad, preferred_element_type=jnp.float32).astype(
            jnp.bfloat16
        )
    )
    return (first_sum, second_out)


def solution(mesh):
    n_blk, n_dp = mesh.devices.shape
    n_core = 2
    split_mesh = Mesh(
        mesh.devices.reshape(n_blk, n_dp // n_core, n_core), ("blk", "ylo", "core")
    )
    dp = ("ylo", "core")
    return jax.shard_map(
        shards,
        mesh=split_mesh,
        in_specs=(P("blk", dp), P("blk", dp), P(dp, "blk", None), P(dp, "blk", None)),
        out_specs=(P(dp, "blk", None), P(dp, "blk", None)),
        check_vma=False,
    )
```

```python
import math

import jax
import jax.numpy as jnp
from jax import lax
from jax.experimental.layout import Layout, with_layout_constraint
from jax.sharding import Mesh
from jax.sharding import PartitionSpec as P

NB = 1024
BS = 256


tanh_scale = 0.7978845608028654
cubic_coef = 0.044715


def gelu_value(values):
    inner = jnp.tanh(tanh_scale * (values + cubic_coef * values * values * values))
    return 0.5 * values * (1.0 + inner)


def gelu_slope(values):
    inner = jnp.tanh(tanh_scale * (values + cubic_coef * values * values * values))
    return 0.5 * (1.0 + inner) + 0.5 * values * (1.0 - inner * inner) * tanh_scale * (
        1.0 + 3.0 * cubic_coef * values * values
    )


def line_pairs(n, step):
    return [(i, i + step) for i in range(n) if 0 <= i + step < n]


def swap_pairs(n):
    return [(c, (c + 1) % n) for c in range(n)]


def swap_pairs(n):
    return [(c, (c + 1) % n) for c in range(n)]


def gather_rows(piece):
    n_core = lax.axis_size("core")
    n_ylo = lax.axis_size("ylo")
    c = lax.axis_index("core")
    y = lax.axis_index("ylo")
    right = [lax.ppermute(piece, "ylo", line_pairs(n_ylo, s)) for s in range(n_ylo - 1, 0, -1)]
    left = [lax.ppermute(piece, "ylo", line_pairs(n_ylo, -s)) for s in range(1, n_ylo)]
    stacked = jnp.stack(right + [piece] + left)
    line = lax.dynamic_slice_in_dim(stacked, n_ylo - 1 - y, n_ylo, axis=0)
    other = lax.ppermute(line, "core", swap_pairs(n_core))
    pair = jnp.zeros((n_ylo, n_core) + piece.shape, piece.dtype)
    pair = lax.dynamic_update_index_in_dim(pair, line, c, 1)
    pair = lax.dynamic_update_index_in_dim(pair, other, lax.rem(c + 1, n_core), 1)
    return pair.reshape((n_ylo * n_core * piece.shape[0],) + piece.shape[1:])


def scatter_rows(term):
    n_core = lax.axis_size("core")
    n_ylo = lax.axis_size("ylo")
    c = lax.axis_index("core")
    blocks, total_rows, width = term.shape
    rows = total_rows // (n_core * n_ylo)
    split = term.reshape(blocks, n_ylo, n_core, rows, width)
    sent = lax.dynamic_index_in_dim(split, lax.rem(c + 1, n_core), 2, keepdims=False)
    kept = lax.dynamic_index_in_dim(split, c, 2, keepdims=False)
    got = lax.ppermute(sent, "core", swap_pairs(n_core))
    half = (kept.astype(jnp.float32) + got.astype(jnp.float32)).astype(jnp.bfloat16)
    arrived = lax.all_to_all(half, "ylo", split_axis=1, concat_axis=1, tiled=True)
    total = jnp.sum(arrived.astype(jnp.float32), axis=1).astype(jnp.bfloat16)
    return jnp.transpose(total, (1, 0, 2))


def shards(input_field, target_field, first_factor, second_factor):
    block_count = first_factor.shape[1]
    block_size = first_factor.shape[2]
    row_count = input_field.shape[1]
    dp = ("ylo", "core")
    replica_count = lax.axis_size("ylo") * lax.axis_size("core")
    blk_count = lax.axis_size("blk")
    group_count = NB // BS
    inner_count = block_count // group_count
    scale_factor = 1.0 / math.sqrt(row_count * replica_count)
    inputs = input_field.reshape(block_count, block_size, row_count)
    first_full = gather_rows(first_factor)
    second_full = lax.all_gather(second_factor, dp, axis=0, tiled=True)
    pre_act = jnp.einsum("bkr,kbi->bir", inputs, first_full, preferred_element_type=jnp.float32)
    pre_split = pre_act.reshape(block_count, blk_count, inner_count, row_count)
    activated = gelu_value(pre_split).astype(jnp.bfloat16)
    slope = jnp.transpose(gelu_slope(pre_split).astype(jnp.bfloat16), (2, 1, 0, 3))
    activated, second_full, slope = lax.optimization_barrier((activated, second_full, slope))
    sending = jnp.transpose(activated, (2, 1, 0, 3))
    sending = with_layout_constraint(sending, Layout((1, 0, 2, 3)))
    received = lax.all_to_all(sending, "blk", split_axis=1, concat_axis=1, tiled=True)
    permuted = received.reshape(block_count, block_size, row_count)
    targets = target_field.reshape(block_count, block_size, row_count)
    second_t = jnp.transpose(second_full, (1, 0, 2))
    predicted = jnp.einsum(
        "qcj,qcr->qjr", second_t, permuted, preferred_element_type=jnp.float32
    )
    residual = ((predicted - targets.astype(jnp.float32)) * scale_factor).astype(jnp.bfloat16)
    permuted_grad = jnp.einsum(
        "qcj,qjr->qcr", second_t, residual, preferred_element_type=jnp.float32
    ).astype(jnp.bfloat16)
    term = jnp.einsum("qcr,qjr->cqj", permuted, residual, preferred_element_type=jnp.float32)
    second_out = lax.psum_scatter(
        term.astype(jnp.bfloat16), dp, scatter_dimension=0, tiled=True
    )
    back = permuted_grad.reshape(inner_count, blk_count, block_count, row_count)
    back = with_layout_constraint(back, Layout((1, 0, 2, 3)))
    activated_grad = lax.all_to_all(back, "blk", split_axis=1, concat_axis=1, tiled=True)
    pre_grad = (activated_grad.astype(jnp.float32) * slope).astype(jnp.bfloat16)
    pre_grad = jnp.transpose(pre_grad, (2, 1, 0, 3)).reshape(block_count, block_size, row_count)
    first_sum = scatter_rows(
        jnp.einsum("bkr,bir->bki", inputs, pre_grad, preferred_element_type=jnp.float32).astype(
            jnp.bfloat16
        )
    )
    return (first_sum, second_out)


def solution(mesh):
    n_blk, n_dp = mesh.devices.shape
    n_core = 2
    split_mesh = Mesh(
        mesh.devices.reshape(n_blk, n_dp // n_core, n_core), ("blk", "ylo", "core")
    )
    dp = ("ylo", "core")
    return jax.shard_map(
        shards,
        mesh=split_mesh,
        in_specs=(P("blk", dp), P("blk", dp), P(dp, "blk", None), P(dp, "blk", None)),
        out_specs=(P(dp, "blk", None), P(dp, "blk", None)),
        check_vma=False,
    )
```

```python
import math

import jax
import jax.numpy as jnp
from jax import lax
from jax.experimental.layout import Layout, with_layout_constraint
from jax.sharding import Mesh
from jax.sharding import PartitionSpec as P

NB = 1024
BS = 256


tanh_scale = 0.7978845608028654
cubic_coef = 0.044715


def gelu_value(values):
    inner = jnp.tanh(tanh_scale * (values + cubic_coef * values * values * values))
    return 0.5 * values * (1.0 + inner)


def gelu_slope(values):
    inner = jnp.tanh(tanh_scale * (values + cubic_coef * values * values * values))
    return 0.5 * (1.0 + inner) + 0.5 * values * (1.0 - inner * inner) * tanh_scale * (
        1.0 + 3.0 * cubic_coef * values * values
    )


def line_pairs(n, step):
    return [(i, i + step) for i in range(n) if 0 <= i + step < n]


def swap_pairs(n):
    return [(c, (c + 1) % n) for c in range(n)]


def swap_pairs(n):
    return [(c, (c + 1) % n) for c in range(n)]


def gather_rows(piece):
    n_core = lax.axis_size("core")
    n_ylo = lax.axis_size("ylo")
    c = lax.axis_index("core")
    copies = jnp.broadcast_to(piece[None], (n_ylo,) + piece.shape)
    line = lax.all_to_all(copies, "ylo", split_axis=0, concat_axis=0, tiled=True)
    other = lax.ppermute(line, "core", swap_pairs(n_core))
    pair = jnp.zeros((n_ylo, n_core) + piece.shape, piece.dtype)
    pair = lax.dynamic_update_index_in_dim(pair, line, c, 1)
    pair = lax.dynamic_update_index_in_dim(pair, other, lax.rem(c + 1, n_core), 1)
    return pair.reshape((n_ylo * n_core * piece.shape[0],) + piece.shape[1:])


def scatter_rows(term):
    n_core = lax.axis_size("core")
    n_ylo = lax.axis_size("ylo")
    c = lax.axis_index("core")
    blocks, total_rows, width = term.shape
    rows = total_rows // (n_core * n_ylo)
    split = term.reshape(blocks, n_ylo, n_core, rows, width)
    sent = lax.dynamic_index_in_dim(split, lax.rem(c + 1, n_core), 2, keepdims=False)
    kept = lax.dynamic_index_in_dim(split, c, 2, keepdims=False)
    got = lax.ppermute(sent, "core", swap_pairs(n_core))
    half = (kept.astype(jnp.float32) + got.astype(jnp.float32)).astype(jnp.bfloat16)
    arrived = lax.all_to_all(half, "ylo", split_axis=1, concat_axis=1, tiled=True)
    total = jnp.sum(arrived.astype(jnp.float32), axis=1).astype(jnp.bfloat16)
    return jnp.transpose(total, (1, 0, 2))


def shards(input_field, target_field, first_factor, second_factor):
    block_count = first_factor.shape[1]
    block_size = first_factor.shape[2]
    row_count = input_field.shape[1]
    dp = ("ylo", "core")
    replica_count = lax.axis_size("ylo") * lax.axis_size("core")
    blk_count = lax.axis_size("blk")
    group_count = NB // BS
    inner_count = block_count // group_count
    scale_factor = 1.0 / math.sqrt(row_count * replica_count)
    inputs = input_field.reshape(block_count, block_size, row_count)
    first_full = gather_rows(first_factor)
    second_full = lax.all_gather(second_factor, dp, axis=0, tiled=True)
    pre_act = jnp.einsum("bkr,kbi->bir", inputs, first_full, preferred_element_type=jnp.float32)
    pre_split = pre_act.reshape(block_count, blk_count, inner_count, row_count)
    activated = gelu_value(pre_split).astype(jnp.bfloat16)
    slope = jnp.transpose(gelu_slope(pre_split).astype(jnp.bfloat16), (2, 1, 0, 3))
    targets = target_field.reshape(block_count, block_size, row_count).astype(jnp.float32)
    activated, second_full, slope, targets = lax.optimization_barrier(
        (activated, second_full, slope, targets)
    )
    sending = jnp.transpose(activated, (2, 1, 0, 3))
    sending = with_layout_constraint(sending, Layout((1, 0, 2, 3)))
    received = lax.all_to_all(sending, "blk", split_axis=1, concat_axis=1, tiled=True)
    permuted = received.reshape(block_count, block_size, row_count)
    second_t = jnp.transpose(second_full, (1, 0, 2))
    predicted = jnp.einsum(
        "qcj,qcr->qjr", second_t, permuted, preferred_element_type=jnp.float32
    )
    residual = ((predicted - targets) * scale_factor).astype(jnp.bfloat16)
    permuted_grad = jnp.einsum(
        "qcj,qjr->qcr", second_t, residual, preferred_element_type=jnp.float32
    ).astype(jnp.bfloat16)
    term = jnp.einsum("qcr,qjr->cqj", permuted, residual, preferred_element_type=jnp.float32)
    second_out = lax.psum_scatter(
        term.astype(jnp.bfloat16), dp, scatter_dimension=0, tiled=True
    )
    back = permuted_grad.reshape(inner_count, blk_count, block_count, row_count)
    back = with_layout_constraint(back, Layout((1, 0, 2, 3)))
    activated_grad = lax.all_to_all(back, "blk", split_axis=1, concat_axis=1, tiled=True)
    pre_grad = (activated_grad.astype(jnp.float32) * slope).astype(jnp.bfloat16)
    pre_grad = jnp.transpose(pre_grad, (2, 1, 0, 3)).reshape(block_count, block_size, row_count)
    first_sum = scatter_rows(
        jnp.einsum("bkr,bir->bki", inputs, pre_grad, preferred_element_type=jnp.float32).astype(
            jnp.bfloat16
        )
    )
    return (first_sum, second_out)


def solution(mesh):
    n_blk, n_dp = mesh.devices.shape
    n_core = 2
    split_mesh = Mesh(
        mesh.devices.reshape(n_blk, n_dp // n_core, n_core), ("blk", "ylo", "core")
    )
    dp = ("ylo", "core")
    return jax.shard_map(
        shards,
        mesh=split_mesh,
        in_specs=(P("blk", dp), P("blk", dp), P(dp, "blk", None), P(dp, "blk", None)),
        out_specs=(P(dp, "blk", None), P(dp, "blk", None)),
        check_vma=False,
    )
```

```python
import math

import jax
import jax.numpy as jnp
from jax import lax
from jax.experimental.layout import Layout, with_layout_constraint
from jax.sharding import Mesh
from jax.sharding import PartitionSpec as P

NB = 1024
BS = 256


tanh_scale = 0.7978845608028654
cubic_coef = 0.044715


def gelu_value(values):
    inner = jnp.tanh(tanh_scale * (values + cubic_coef * values * values * values))
    return 0.5 * values * (1.0 + inner)


def gelu_slope(values):
    inner = jnp.tanh(tanh_scale * (values + cubic_coef * values * values * values))
    return 0.5 * (1.0 + inner) + 0.5 * values * (1.0 - inner * inner) * tanh_scale * (
        1.0 + 3.0 * cubic_coef * values * values
    )


def line_pairs(n, step):
    return [(i, i + step) for i in range(n) if 0 <= i + step < n]


def swap_pairs(n):
    return [(c, (c + 1) % n) for c in range(n)]


def swap_pairs(n):
    return [(c, (c + 1) % n) for c in range(n)]


def gather_rows(piece):
    n_core = lax.axis_size("core")
    n_ylo = lax.axis_size("ylo")
    c = lax.axis_index("core")
    copies = jnp.broadcast_to(piece[None], (n_ylo,) + piece.shape)
    line = lax.all_to_all(copies, "ylo", split_axis=0, concat_axis=0, tiled=True)
    other = lax.ppermute(line, "core", swap_pairs(n_core))
    pair = jnp.zeros((n_ylo, n_core) + piece.shape, piece.dtype)
    pair = lax.dynamic_update_index_in_dim(pair, line, c, 1)
    pair = lax.dynamic_update_index_in_dim(pair, other, lax.rem(c + 1, n_core), 1)
    return pair.reshape((n_ylo * n_core * piece.shape[0],) + piece.shape[1:])


def scatter_rows(inputs, pre_grad):
    n_core = lax.axis_size("core")
    n_ylo = lax.axis_size("ylo")
    c = lax.axis_index("core")
    blocks, total_rows, width = inputs.shape
    rows = total_rows // (n_core * n_ylo)
    split = inputs.reshape(blocks, n_ylo, n_core, rows, width)
    x_other = lax.dynamic_index_in_dim(split, lax.rem(c + 1, n_core), 2, keepdims=False)
    x_mine = lax.dynamic_index_in_dim(split, c, 2, keepdims=False)
    sent = jnp.einsum(
        "bykr,bir->byki", x_other, pre_grad, preferred_element_type=jnp.float32
    ).astype(jnp.bfloat16)
    got = lax.ppermute(sent, "core", swap_pairs(n_core))
    kept = jnp.einsum(
        "bykr,bir->byki", x_mine, pre_grad, preferred_element_type=jnp.float32
    ).astype(jnp.bfloat16)
    kept, got = lax.optimization_barrier((kept, got))
    half = (kept.astype(jnp.float32) + got.astype(jnp.float32)).astype(jnp.bfloat16)
    half = with_layout_constraint(half, Layout((1, 0, 2, 3)))
    arrived = lax.all_to_all(half, "ylo", split_axis=1, concat_axis=1, tiled=True)
    total = jnp.sum(arrived.astype(jnp.float32), axis=1).astype(jnp.bfloat16)
    return jnp.transpose(total, (1, 0, 2))


def shards(input_field, target_field, first_factor, second_factor):
    block_count = first_factor.shape[1]
    block_size = first_factor.shape[2]
    row_count = input_field.shape[1]
    dp = ("ylo", "core")
    replica_count = lax.axis_size("ylo") * lax.axis_size("core")
    blk_count = lax.axis_size("blk")
    group_count = NB // BS
    inner_count = block_count // group_count
    scale_factor = 1.0 / math.sqrt(row_count * replica_count)
    inputs = input_field.reshape(block_count, block_size, row_count)
    first_full = gather_rows(first_factor)
    second_full = lax.all_gather(second_factor, dp, axis=0, tiled=True)
    pre_act = jnp.einsum("bkr,kbi->bir", inputs, first_full, preferred_element_type=jnp.float32)
    pre_split = pre_act.reshape(block_count, blk_count, inner_count, row_count)
    activated = gelu_value(pre_split).astype(jnp.bfloat16)
    slope = jnp.transpose(gelu_slope(pre_split).astype(jnp.bfloat16), (2, 1, 0, 3))
    activated, second_full, slope = lax.optimization_barrier((activated, second_full, slope))
    sending = jnp.transpose(activated, (2, 1, 0, 3))
    sending = with_layout_constraint(sending, Layout((1, 0, 2, 3)))
    received = lax.all_to_all(sending, "blk", split_axis=1, concat_axis=1, tiled=True)
    permuted = received.reshape(block_count, block_size, row_count)
    targets = target_field.reshape(block_count, block_size, row_count)
    second_t = jnp.transpose(second_full, (1, 0, 2))
    predicted = jnp.einsum(
        "qcj,qcr->qjr", second_t, permuted, preferred_element_type=jnp.float32
    )
    residual = ((predicted - targets.astype(jnp.float32)) * scale_factor).astype(jnp.bfloat16)
    permuted_grad = jnp.einsum(
        "qcj,qjr->qcr", second_t, residual, preferred_element_type=jnp.float32
    ).astype(jnp.bfloat16)
    term = jnp.einsum("qcr,qjr->cqj", permuted, residual, preferred_element_type=jnp.float32)
    second_out = lax.psum_scatter(
        term.astype(jnp.bfloat16), dp, scatter_dimension=0, tiled=True
    )
    back = permuted_grad.reshape(inner_count, blk_count, block_count, row_count)
    back = with_layout_constraint(back, Layout((1, 0, 2, 3)))
    activated_grad = lax.all_to_all(back, "blk", split_axis=1, concat_axis=1, tiled=True)
    pre_grad = (activated_grad.astype(jnp.float32) * slope).astype(jnp.bfloat16)
    pre_grad = jnp.transpose(pre_grad, (2, 1, 0, 3)).reshape(block_count, block_size, row_count)
    first_sum = scatter_rows(inputs, pre_grad)
    return (first_sum, second_out)


def solution(mesh):
    n_blk, n_dp = mesh.devices.shape
    n_core = 2
    split_mesh = Mesh(
        mesh.devices.reshape(n_blk, n_dp // n_core, n_core), ("blk", "ylo", "core")
    )
    dp = ("ylo", "core")
    return jax.shard_map(
        shards,
        mesh=split_mesh,
        in_specs=(P("blk", dp), P("blk", dp), P(dp, "blk", None), P(dp, "blk", None)),
        out_specs=(P(dp, "blk", None), P(dp, "blk", None)),
        check_vma=False,
    )
```
